512 devices in a mesh: group: 32 (over y, x), member: 16 (over z, core).
Axes of the slice: x: 4, y: 8, z: 8, core: 2. Of those that a mesh axis runs over, the one named last changes fastest.
Arguments:
- feats: bfloat16 [262144, 1024], P(('group', 'member')), may hold values from -24 to 24
- transform: bfloat16 [1024, 1024], replicated, may hold values from -0.1875 to 0.1875
- bias: float32 [1024], replicated, may hold values from -3 to 3
- tile_list: int32 [2048, 8], P(('group', 'member')), may hold values from 0 to 255, as said below
- nbr_slot: int32 [262144, 16], P(('group', 'member')), may hold values from 0 to 255
- nbr_weight: int32 [262144, 16], P(('group', 'member')), may hold values from 1 to 16
- cotangent: bfloat16 [262144, 1024], P(('group', 'member')), may hold values from -6 to 6
Outputs:
- embedding: bfloat16 [262144, 1024], P(('group', 'member'))
- feat_grad: bfloat16 [262144, 1024], P(('group', 'member'))
- transform_grad: float32 [1024, 1024], P('member')
The draws below stay inside these ranges and needn't reach their ends.
Inputs may be any that keep to these rules, and one draw needn't show every extreme that they name: `tile_list`: each block lists 8 different tiles of its own group; group tile g lies on member g // 16 of that group. Over all blocks of one device, the tiles that lie on another member are at most one distinct tile for each such member.
All inputs are finite; a program needn't handle non-finite values.
Results may differ from the reference program's by a relative error of at most 0.013.
Values may be sent and summed in bfloat16 or wider, within the bound.
No kernel may reach another device: no remote copies, remote signals or barrier semaphores. Data moves between devices by JAX's collectives and lax.ppermute only.
A program may use at most 64 MiB of HBM per device.

```python
import math
import jax
import jax.numpy as jnp
from jax import lax

D = 1024
HID = 1024
BLOCK = 128
TILE = 32
K = 8
NBR = 16
BLK_DEV = 4
NODES = 262144
N_GROUP = 32
N_MEMBER = 16


def draw_tile_list(key, part):
    devices = N_GROUP * N_MEMBER
    tiles_dev = BLK_DEV * BLOCK // TILE
    breadth = tiles_dev + N_MEMBER
    key_pick = jax.random.fold_in(key, 11)
    key_rank = jax.random.fold_in(key, 12)
    member = jnp.arange(devices, dtype=jnp.int32) % N_MEMBER
    peer_index = jnp.arange(N_MEMBER, dtype=jnp.int32)
    peer_tile = jax.random.randint(key_pick, (devices, N_MEMBER), 0, tiles_dev, dtype=jnp.int32)
    foreign_ids = peer_index[None, :] * tiles_dev + peer_tile
    own_ids = member[:, None] * tiles_dev + jnp.arange(tiles_dev, dtype=jnp.int32)[None, :]
    candidates = jnp.concatenate([own_ids, foreign_ids], axis=1)
    usable = jnp.concatenate([jnp.ones((devices, tiles_dev), dtype=bool), peer_index[None, :] != member[:, None]], axis=1)
    candidates = jnp.repeat(candidates, BLK_DEV, axis=0)
    usable = jnp.repeat(usable, BLK_DEV, axis=0)
    scores = jax.random.randint(key_rank, (devices * BLK_DEV, breadth), 0, 1 << 20, dtype=jnp.int32) * breadth
    scores = scores + jnp.arange(breadth, dtype=jnp.int32)[None, :]
    scores = jnp.where(usable, scores, -1)
    _, ranked = lax.top_k(scores, K)
    return jnp.take_along_axis(candidates, ranked, axis=1).astype(jnp.int32)


def with_ends(drawn, rng, low, top_value):
    index_at = [jax.random.randint(jax.random.fold_in(rng, axis), (), 0, length) for axis, length in enumerate(drawn.shape)]
    widest = drawn.shape.index(max(drawn.shape))
    neighbour = index_at[:widest] + [(index_at[widest] + 1) % drawn.shape[widest]] + index_at[widest + 1:]
    return drawn.at[tuple(index_at)].set(low).at[tuple(neighbour)].set(top_value)


def with_spikes(drawn, key, source, target, blocks, factor):
    owner, partner = [(jnp.arange(drawn.shape[position]) // (drawn.shape[position] // blocks)).reshape([-1 if axis == position else 1 for axis in range(drawn.ndim)]) for position in (source, target)]
    chosen = jax.random.permutation(key, blocks)[partner]
    strong = (owner == chosen) | (owner == (partner + blocks // 2) % blocks)
    return jnp.where(strong, factor * drawn, drawn)


def levels(key, shape, split, smallest, largest):
    def one(position, shards_of):
        draws = jax.random.uniform(jax.random.fold_in(jax.random.fold_in(key, 6), position), (shards_of,), jnp.float32, smallest / len(split), largest / len(split))
        return jnp.repeat(jnp.exp(draws), shape[position] // shards_of).reshape((-1,) + (1,) * (len(shape) - position - 1))

    factor_of = one(*split[0])
    for cut in split[1:]:
        factor_of = factor_of * one(*cut)
    return factor_of


def scatter_about(rng, shape, width, most, pieces=(), kind=jnp.bfloat16):
    result = width * jax.random.normal(rng, shape, jnp.float32)
    if pieces:
        result = result * levels(rng, shape, pieces, -0.22, 0.18)
    return jnp.clip(result, -most, most).astype(kind)


def bell_draw_with(key, dims, spread, reach, split, heavy, held_as=jnp.bfloat16):
    entries = spread * jax.random.normal(key, dims, jnp.float32)
    if split:
        entries = entries * levels(key, dims, split, -0.22, 0.18)
    return jnp.clip(with_spikes(entries, jax.random.fold_in(key, 3), *heavy), -reach, reach).astype(held_as)


def setup_inputs(seed: int = 0) -> dict:
    streams_of = jax.random.split(jax.random.key(seed), 8)
    feats = bell_draw_with(streams_of[0], (NODES, D), 1.0, 24.0, ((0, 512),), (0, 1, 512, 6.0))
    transform = scatter_about(streams_of[1], (D, HID), D ** -0.5, 0.1875)
    bias = scatter_about(streams_of[2], (HID,), 0.5, 3.0, (), jnp.float32)
    tile_list = draw_tile_list(jax.random.fold_in(streams_of[7], 71), 0)
    nbr_slot = with_ends(jax.random.randint(streams_of[4], (NODES, NBR), 0, K * TILE), jax.random.fold_in(streams_of[4], 1), 0, (K * TILE) - 1).astype(jnp.int32)
    nbr_weight = with_ends(jax.random.randint(streams_of[5], (NODES, NBR), 1, 17), jax.random.fold_in(streams_of[5], 1), 1, 16).astype(jnp.int32)
    cotangent = scatter_about(streams_of[6], (NODES, HID), 1.0, 6.0, ((0, 512),))
    return {"feats": feats, "transform": transform, "bias": bias, "tile_list": tile_list, "nbr_slot": nbr_slot, "nbr_weight": nbr_weight, "cotangent": cotangent}


def adjacency_of(slot_rows, weights, cand_width):
    columns = lax.broadcasted_iota(jnp.int32, slot_rows.shape + (cand_width,), slot_rows.ndim)
    matched_weights = jnp.where(slot_rows[..., None] == columns, weights[..., None], 0)
    return lax.optimization_barrier(jnp.sum(matched_weights, axis=-2)).astype(jnp.bfloat16)

def reference(feats, transform, bias, tile_list, nbr_slot, nbr_weight, cotangent):
    rows_dev = BLK_DEV * BLOCK
    devices = N_GROUP * N_MEMBER
    tiles_dev = rows_dev // TILE
    cand_width = K * TILE
    preact = jnp.dot(feats, transform, preferred_element_type=jnp.float32) + bias
    message = jnp.maximum(preact, 0.0).astype(jnp.bfloat16)
    all_tiles = message.reshape(devices * tiles_dev, TILE, HID)
    block_group = jnp.arange(devices * BLK_DEV, dtype=jnp.int32) // (BLK_DEV * N_MEMBER)
    global_ids = (tile_list + (block_group * (N_MEMBER * tiles_dev))[:, None]).astype(jnp.int32)
    ids_dev = global_ids.reshape(devices, BLK_DEV * K)
    slot_rows = nbr_slot.reshape(devices, BLK_DEV, BLOCK, NBR)
    weights = nbr_weight.reshape(devices, BLK_DEV, BLOCK, NBR)
    own_rows = message.reshape(devices, BLK_DEV, BLOCK, HID)
    upstream = cotangent.reshape(devices, BLK_DEV, BLOCK, HID)

    def device_step(collected, inputs):
        device, tile_ids, slot_here, weight_here, own_here, incoming_raw = inputs
        adjacency = adjacency_of(slot_here, weight_here, cand_width)
        candidates = all_tiles[tile_ids].reshape(BLK_DEV, cand_width, HID)
        weight_total = lax.optimization_barrier(jnp.sum(weight_here, axis=2)).astype(jnp.float32)[..., None]
        gathered = jnp.einsum('brc,bch->brh', adjacency.astype(jnp.float32), candidates.astype(jnp.float32))
        combined = gathered / weight_total + own_here.astype(jnp.float32)
        inv_rms = lax.rsqrt(lax.optimization_barrier(jnp.mean(combined * combined, axis=2, keepdims=True)) + 1e-06)
        normed = combined * inv_rms
        incoming = incoming_raw.astype(jnp.float32)
        mixed_grad = inv_rms * (incoming - normed * lax.optimization_barrier(jnp.mean(incoming * normed, axis=2, keepdims=True)))
        agg_grad = (mixed_grad / weight_total).astype(jnp.bfloat16)
        cand_grad = jnp.einsum('brc,brh->bch', adjacency.astype(jnp.float32), agg_grad.astype(jnp.float32))
        cand_grad = cand_grad.reshape(BLK_DEV * K, TILE, HID)
        matches = (tile_ids[:, None] == tile_ids[None, :]).astype(jnp.float32)
        summed = jnp.einsum('ij,jth->ith', matches, cand_grad, precision=lax.Precision.HIGHEST)
        earlier = lax.optimization_barrier(jnp.sum(jnp.tril(matches, -1), axis=1))
        leading = (earlier == 0.0).astype(jnp.float32)
        holder = tile_ids // tiles_dev
        foreign = holder != device
        rounded = lax.optimization_barrier(summed.astype(jnp.bfloat16)).astype(jnp.float32)
        returned = jnp.where(foreign[:, None, None], rounded, summed) * leading[:, None, None]
        collected = collected.at[tile_ids].add(returned)
        return (collected, (normed.astype(jnp.bfloat16), mixed_grad))
    initial = jnp.zeros((devices * tiles_dev, TILE, HID), jnp.float32)
    device_ids = jnp.arange(devices, dtype=jnp.int32)
    collected, (embedded, self_grad) = lax.scan(device_step, initial, (device_ids, ids_dev, slot_rows, weights, own_rows, upstream))
    message_grad = self_grad.reshape(NODES, HID) + collected.reshape(NODES, HID)
    pre_grad = jnp.where(preact > 0, message_grad, 0.0).astype(jnp.bfloat16)
    feat_grad = jnp.dot(pre_grad, transform.T, preferred_element_type=jnp.float32).astype(jnp.bfloat16)
    transform_grad = jnp.dot(feats.T, pre_grad, preferred_element_type=jnp.float32) * (1.0 / math.sqrt(NODES))
    return (embedded.reshape(NODES, HID), feat_grad, transform_grad)
```

```python
import math

import jax
import jax.numpy as jnp
from jax import lax
from jax.sharding import PartitionSpec as P

TILE = 32


def adjacency_of(slot_rows, weights, cand_width):
    columns = lax.broadcasted_iota(jnp.int32, slot_rows.shape + (cand_width,), slot_rows.ndim)
    matched_weights = jnp.where(slot_rows[..., None] == columns, weights[..., None], 0)
    return jnp.sum(matched_weights, axis=-2).astype(jnp.bfloat16)


def xor_pairs(n, bit):
    return [(i, i ^ (1 << bit)) for i in range(n)]


def reduce_rows(part):
    members = lax.axis_size("member")
    groups = lax.axis_size("group")
    member_here = lax.axis_index("member")
    rows, cols = part.shape
    acc = part.reshape(members, rows // members, cols)
    for k in range(members.bit_length() - 1):
        pairs = acc.reshape(acc.shape[0] // 2, 2, *acc.shape[1:])
        bit = (member_here >> k) & 1
        keep = lax.dynamic_index_in_dim(pairs, bit, 1, keepdims=False)
        send = lax.dynamic_index_in_dim(pairs, 1 - bit, 1, keepdims=False)
        acc = keep + lax.ppermute(send, "member", xor_pairs(members, k))
    acc = acc.reshape(rows // members, cols)
    for k in range(groups.bit_length() - 1):
        acc = acc + lax.ppermute(acc, "group", xor_pairs(groups, k))
    return acc


def on_device(feats, transform, bias, tile_list, nbr_slot, nbr_weight, cotangent):
    rows_dev, feat_width = feats.shape
    hidden_width = transform.shape[1]
    blocks, tiles_per = tile_list.shape
    block_rows = rows_dev // blocks
    members = lax.axis_size("member")
    groups = lax.axis_size("group")
    member_here = lax.axis_index("member")
    tiles_dev = rows_dev // TILE
    cand_width = tiles_per * TILE
    preact = jnp.dot(feats, transform, preferred_element_type=jnp.float32) + bias
    message = jnp.maximum(preact, 0.0).astype(jnp.bfloat16)
    own_tiles = message.reshape(tiles_dev, TILE, hidden_width)
    holder = tile_list // tiles_dev
    local_index = tile_list % tiles_dev
    foreign = holder != member_here
    peer_ids = lax.broadcasted_iota(jnp.int32, (1, 1, members), 2)
    matched = (holder[..., None] == peer_ids) & foreign[..., None]
    wanted = jnp.max(jnp.where(matched, local_index[..., None], -1), axis=(0, 1))
    asked_for = lax.all_to_all(
        wanted.reshape(members, 1), "member", split_axis=0, concat_axis=0, tiled=True
    )[:, 0]
    served = jnp.clip(asked_for, 0, tiles_dev - 1)
    remote = lax.all_to_all(own_tiles[served], "member", split_axis=0, concat_axis=0, tiled=True)
    tile_pool = jnp.concatenate([remote, own_tiles], axis=0)
    pool_index = jnp.where(foreign, holder, members + local_index).reshape(-1)
    candidates = tile_pool[pool_index].reshape(blocks, cand_width, hidden_width)
    slot_rows = nbr_slot.reshape(blocks, block_rows, -1)
    weights = nbr_weight.reshape(blocks, block_rows, -1)
    adjacency = adjacency_of(slot_rows, weights, cand_width)
    weight_total = jnp.sum(weights, axis=2).astype(jnp.float32)[..., None]
    gathered = jnp.einsum("brc,bch->brh", adjacency, candidates, preferred_element_type=jnp.float32)
    combined = gathered / weight_total + message.reshape(blocks, block_rows, hidden_width).astype(
        jnp.float32
    )
    inv_rms = lax.rsqrt(jnp.mean(combined * combined, axis=2, keepdims=True) + 1e-06)
    normed = combined * inv_rms
    embedding = normed.astype(jnp.bfloat16).reshape(rows_dev, hidden_width)
    incoming = cotangent.reshape(blocks, block_rows, hidden_width).astype(jnp.float32)
    mixed_grad = inv_rms * (incoming - normed * jnp.mean(incoming * normed, axis=2, keepdims=True))
    agg_grad = (mixed_grad / weight_total).astype(jnp.bfloat16)
    cand_grad = jnp.einsum("brc,brh->bch", adjacency, agg_grad, preferred_element_type=jnp.float32)
    cand_grad = cand_grad.reshape(blocks * tiles_per, TILE, hidden_width)
    pool_size = members + tiles_dev
    pool_grad = jax.ops.segment_sum(cand_grad, pool_index, num_segments=pool_size)
    returned = pool_grad[:members].astype(jnp.bfloat16)
    came_back = lax.all_to_all(returned, "member", split_axis=0, concat_axis=0, tiled=True)
    back_rows = jnp.where((asked_for >= 0)[:, None, None], came_back.astype(jnp.float32), 0.0)
    tile_grad = pool_grad[members:].at[served].add(back_rows)
    message_grad = mixed_grad.reshape(rows_dev, hidden_width) + tile_grad.reshape(
        rows_dev, hidden_width
    )
    pre_grad = jnp.where(preact > 0, message_grad, 0.0).astype(jnp.bfloat16)
    feat_grad = lax.dot_general(
        pre_grad, transform, (((1,), (1,)), ((), ())), preferred_element_type=jnp.float32
    ).astype(jnp.bfloat16)
    partial = lax.dot_general(
        feats, pre_grad, (((0,), (0,)), ((), ())), preferred_element_type=jnp.float32
    )
    factor = 1.0 / math.sqrt(rows_dev * members * groups)
    transform_grad = reduce_rows(partial) * factor
    return (embedding, feat_grad, transform_grad)


def solution(mesh):
    return jax.shard_map(
        on_device,
        mesh=mesh,
        in_specs=(
            P(("group", "member"), None),
            P(),
            P(),
            P(("group", "member"), None),
            P(("group", "member"), None),
            P(("group", "member"), None),
            P(("group", "member"), None),
        ),
        out_specs=(P(("group", "member"), None), P(("group", "member"), None), P("member", None)),
        check_vma=False,
    )
```

```python
import math

import jax
import jax.numpy as jnp
from jax import lax
from jax.sharding import PartitionSpec as P

TILE = 32


def adjacency_of(slot_rows, weights, cand_width):
    columns = lax.broadcasted_iota(jnp.int32, slot_rows.shape + (cand_width,), slot_rows.ndim)
    matched_weights = jnp.where(slot_rows[..., None] == columns, weights[..., None], 0)
    return jnp.sum(matched_weights, axis=-2).astype(jnp.bfloat16)


def xor_pairs(n, bit):
    return [(i, i ^ (1 << bit)) for i in range(n)]


def reduce_rows(part):
    members = lax.axis_size("member")
    groups = lax.axis_size("group")
    member_here = lax.axis_index("member")
    rows, cols = part.shape
    acc = part.reshape(members, rows // members, cols)
    for k in range(members.bit_length() - 1):
        pairs = acc.reshape(acc.shape[0] // 2, 2, *acc.shape[1:])
        bit = (member_here >> k) & 1
        keep = lax.dynamic_index_in_dim(pairs, bit, 1, keepdims=False)
        send = lax.dynamic_index_in_dim(pairs, 1 - bit, 1, keepdims=False)
        sent = lax.ppermute(send.astype(jnp.bfloat16), "member", xor_pairs(members, k))
        acc = keep + sent.astype(jnp.float32)
    acc = acc.reshape(rows // members, cols)
    for k in range(groups.bit_length() - 1):
        mine = acc.astype(jnp.bfloat16)
        theirs = lax.ppermute(mine, "group", xor_pairs(groups, k))
        acc = mine.astype(jnp.float32) + theirs.astype(jnp.float32)
    return acc


def on_device(feats, transform, bias, tile_list, nbr_slot, nbr_weight, cotangent):
    rows_dev, feat_width = feats.shape
    hidden_width = transform.shape[1]
    blocks, tiles_per = tile_list.shape
    block_rows = rows_dev // blocks
    members = lax.axis_size("member")
    groups = lax.axis_size("group")
    member_here = lax.axis_index("member")
    tiles_dev = rows_dev // TILE
    cand_width = tiles_per * TILE
    preact = jnp.dot(feats, transform, preferred_element_type=jnp.float32) + bias
    message = jnp.maximum(preact, 0.0).astype(jnp.bfloat16)
    own_tiles = message.reshape(tiles_dev, TILE, hidden_width)
    holder = tile_list // tiles_dev
    local_index = tile_list % tiles_dev
    foreign = holder != member_here
    peer_ids = lax.broadcasted_iota(jnp.int32, (1, 1, members), 2)
    matched = (holder[..., None] == peer_ids) & foreign[..., None]
    wanted = jnp.max(jnp.where(matched, local_index[..., None], -1), axis=(0, 1))
    asked_for = lax.all_to_all(
        wanted.reshape(members, 1), "member", split_axis=0, concat_axis=0, tiled=True
    )[:, 0]
    served = jnp.clip(asked_for, 0, tiles_dev - 1)
    remote = lax.all_to_all(own_tiles[served], "member", split_axis=0, concat_axis=0, tiled=True)
    tile_pool = jnp.concatenate([remote, own_tiles], axis=0)
    pool_index = jnp.where(foreign, holder, members + local_index).reshape(-1)
    candidates = tile_pool[pool_index].reshape(blocks, cand_width, hidden_width)
    slot_rows = nbr_slot.reshape(blocks, block_rows, -1)
    weights = nbr_weight.reshape(blocks, block_rows, -1)
    adjacency = adjacency_of(slot_rows, weights, cand_width)
    weight_total = jnp.sum(weights, axis=2).astype(jnp.float32)[..., None]
    gathered = jnp.einsum("brc,bch->brh", adjacency, candidates, preferred_element_type=jnp.float32)
    combined = gathered / weight_total + message.reshape(blocks, block_rows, hidden_width).astype(
        jnp.float32
    )
    inv_rms = lax.rsqrt(jnp.mean(combined * combined, axis=2, keepdims=True) + 1e-06)
    normed = combined * inv_rms
    embedding = normed.astype(jnp.bfloat16).reshape(rows_dev, hidden_width)
    incoming = cotangent.reshape(blocks, block_rows, hidden_width).astype(jnp.float32)
    mixed_grad = inv_rms * (incoming - normed * jnp.mean(incoming * normed, axis=2, keepdims=True))
    agg_grad = (mixed_grad / weight_total).astype(jnp.bfloat16)
    cand_grad = jnp.einsum("brc,brh->bch", adjacency, agg_grad, preferred_element_type=jnp.float32)
    cand_grad = cand_grad.reshape(blocks * tiles_per, TILE, hidden_width)
    pool_size = members + tiles_dev
    pool_grad = jax.ops.segment_sum(cand_grad, pool_index, num_segments=pool_size)
    returned = pool_grad[:members].astype(jnp.bfloat16)
    came_back = lax.all_to_all(returned, "member", split_axis=0, concat_axis=0, tiled=True)
    back_rows = jnp.where((asked_for >= 0)[:, None, None], came_back.astype(jnp.float32), 0.0)
    tile_grad = pool_grad[members:].at[served].add(back_rows)
    message_grad = mixed_grad.reshape(rows_dev, hidden_width) + tile_grad.reshape(
        rows_dev, hidden_width
    )
    pre_grad = jnp.where(preact > 0, message_grad, 0.0).astype(jnp.bfloat16)
    feat_grad = lax.dot_general(
        pre_grad, transform, (((1,), (1,)), ((), ())), preferred_element_type=jnp.float32
    ).astype(jnp.bfloat16)
    partial = lax.dot_general(
        feats, pre_grad, (((0,), (0,)), ((), ())), preferred_element_type=jnp.float32
    )
    factor = 1.0 / math.sqrt(rows_dev * members * groups)
    transform_grad = reduce_rows(partial) * factor
    return (embedding, feat_grad, transform_grad)


def solution(mesh):
    return jax.shard_map(
        on_device,
        mesh=mesh,
        in_specs=(
            P(("group", "member"), None),
            P(),
            P(),
            P(("group", "member"), None),
            P(("group", "member"), None),
            P(("group", "member"), None),
            P(("group", "member"), None),
        ),
        out_specs=(P(("group", "member"), None), P(("group", "member"), None), P("member", None)),
        check_vma=False,
    )
```

```python
import math

import jax
import jax.numpy as jnp
from jax import lax
from jax.sharding import PartitionSpec as P

TILE = 32


def adjacency_of(slot_rows, weights, cand_width):
    columns = lax.broadcasted_iota(jnp.int32, slot_rows.shape + (cand_width,), slot_rows.ndim)
    matched_weights = jnp.where(slot_rows[..., None] == columns, weights[..., None], 0)
    return jnp.sum(matched_weights, axis=-2).astype(jnp.bfloat16)


def xor_pairs(n, bit):
    return [(i, i ^ (1 << bit)) for i in range(n)]


def shifted_pairs(members, bit):
    chips = members // 2
    pairs = []
    for m in range(members):
        chip, core = divmod(m, 2)
        label = ((chip - core) % chips) ^ (1 << bit)
        pairs.append((m, 2 * ((label + core) % chips) + core))
    return pairs


def halve(acc, bit):
    pairs = acc.reshape(acc.shape[0] // 2, 2, *acc.shape[1:])
    keep = lax.dynamic_index_in_dim(pairs, bit, 1, keepdims=False)
    send = lax.dynamic_index_in_dim(pairs, 1 - bit, 1, keepdims=False)
    return keep, send


def reduce_rows(part):
    members = lax.axis_size("member")
    groups = lax.axis_size("group")
    member_here = lax.axis_index("member")
    chips = members // 2
    chip, core = member_here // 2, member_here % 2
    rows, cols = part.shape
    acc = part.reshape(members, rows // members, cols)
    keep, send = halve(acc, core)
    sent = lax.ppermute(send.astype(jnp.bfloat16), "member", xor_pairs(members, 0))
    acc = keep + sent.astype(jnp.float32)
    acc = lax.dynamic_slice_in_dim(jnp.concatenate([acc, acc], axis=0), core, chips, 0)
    label = (chip - core) % chips
    for k in range(chips.bit_length() - 1):
        keep, send = halve(acc, (label >> k) & 1)
        sent = lax.ppermute(send.astype(jnp.bfloat16), "member", shifted_pairs(members, k))
        acc = keep + sent.astype(jnp.float32)
    acc = acc.reshape(rows // members, cols)
    for k in range(groups.bit_length() - 1):
        acc = acc + lax.ppermute(acc, "group", xor_pairs(groups, k))
    return acc


def on_device(feats, transform, bias, tile_list, nbr_slot, nbr_weight, cotangent):
    rows_dev, feat_width = feats.shape
    hidden_width = transform.shape[1]
    blocks, tiles_per = tile_list.shape
    block_rows = rows_dev // blocks
    members = lax.axis_size("member")
    groups = lax.axis_size("group")
    member_here = lax.axis_index("member")
    tiles_dev = rows_dev // TILE
    cand_width = tiles_per * TILE
    preact = jnp.dot(feats, transform, preferred_element_type=jnp.float32) + bias
    message = jnp.maximum(preact, 0.0).astype(jnp.bfloat16)
    own_tiles = message.reshape(tiles_dev, TILE, hidden_width)
    holder = tile_list // tiles_dev
    local_index = tile_list % tiles_dev
    foreign = holder != member_here
    peer_ids = lax.broadcasted_iota(jnp.int32, (1, 1, members), 2)
    matched = (holder[..., None] == peer_ids) & foreign[..., None]
    wanted = jnp.max(jnp.where(matched, local_index[..., None], -1), axis=(0, 1))
    asked_for = lax.all_to_all(
        wanted.reshape(members, 1), "member", split_axis=0, concat_axis=0, tiled=True
    )[:, 0]
    served = jnp.clip(asked_for, 0, tiles_dev - 1)
    remote = lax.all_to_all(own_tiles[served], "member", split_axis=0, concat_axis=0, tiled=True)
    tile_pool = jnp.concatenate([remote, own_tiles], axis=0)
    pool_index = jnp.where(foreign, holder, members + local_index).reshape(-1)
    candidates = tile_pool[pool_index].reshape(blocks, cand_width, hidden_width)
    slot_rows = nbr_slot.reshape(blocks, block_rows, -1)
    weights = nbr_weight.reshape(blocks, block_rows, -1)
    adjacency = adjacency_of(slot_rows, weights, cand_width)
    weight_total = jnp.sum(weights, axis=2).astype(jnp.float32)[..., None]
    gathered = jnp.einsum("brc,bch->brh", adjacency, candidates, preferred_element_type=jnp.float32)
    combined = gathered / weight_total + message.reshape(blocks, block_rows, hidden_width).astype(
        jnp.float32
    )
    inv_rms = lax.rsqrt(jnp.mean(combined * combined, axis=2, keepdims=True) + 1e-06)
    normed = combined * inv_rms
    embedding = normed.astype(jnp.bfloat16).reshape(rows_dev, hidden_width)
    incoming = cotangent.reshape(blocks, block_rows, hidden_width).astype(jnp.float32)
    mixed_grad = inv_rms * (incoming - normed * jnp.mean(incoming * normed, axis=2, keepdims=True))
    agg_grad = (mixed_grad / weight_total).astype(jnp.bfloat16)
    cand_grad = jnp.einsum("brc,brh->bch", adjacency, agg_grad, preferred_element_type=jnp.float32)
    cand_grad = cand_grad.reshape(blocks * tiles_per, TILE, hidden_width)
    pool_size = members + tiles_dev
    pool_grad = jax.ops.segment_sum(cand_grad, pool_index, num_segments=pool_size)
    returned = pool_grad[:members].astype(jnp.bfloat16)
    came_back = lax.all_to_all(returned, "member", split_axis=0, concat_axis=0, tiled=True)
    back_rows = jnp.where((asked_for >= 0)[:, None, None], came_back.astype(jnp.float32), 0.0)
    tile_grad = pool_grad[members:].at[served].add(back_rows)
    message_grad = mixed_grad.reshape(rows_dev, hidden_width) + tile_grad.reshape(
        rows_dev, hidden_width
    )
    pre_grad = jnp.where(preact > 0, message_grad, 0.0).astype(jnp.bfloat16)
    feat_grad = lax.dot_general(
        pre_grad, transform, (((1,), (1,)), ((), ())), preferred_element_type=jnp.float32
    ).astype(jnp.bfloat16)
    partial = lax.dot_general(
        feats, pre_grad, (((0,), (0,)), ((), ())), preferred_element_type=jnp.float32
    )
    factor = 1.0 / math.sqrt(rows_dev * members * groups)
    transform_grad = reduce_rows(partial) * factor
    return (embedding, feat_grad, transform_grad)


def solution(mesh):
    return jax.shard_map(
        on_device,
        mesh=mesh,
        in_specs=(
            P(("group", "member"), None),
            P(),
            P(),
            P(("group", "member"), None),
            P(("group", "member"), None),
            P(("group", "member"), None),
            P(("group", "member"), None),
        ),
        out_specs=(P(("group", "member"), None), P(("group", "member"), None), P("member", None)),
        check_vma=False,
    )
```

```python
import math

import jax
import jax.numpy as jnp
from jax import lax
from jax.sharding import PartitionSpec as P

TILE = 32
GROUP_MINOR = 4


def adjacency_of(slot_rows, weights, cand_width):
    columns = lax.broadcasted_iota(jnp.int32, slot_rows.shape + (cand_width,), slot_rows.ndim)
    matched_weights = jnp.where(slot_rows[..., None] == columns, weights[..., None], 0)
    return jnp.sum(matched_weights, axis=-2).astype(jnp.bfloat16)


def xor_pairs(n, bit):
    return [(i, i ^ (1 << bit)) for i in range(n)]


def shifted_pairs(members, bit):
    chips = members // 2
    pairs = []
    for m in range(members):
        chip, core = divmod(m, 2)
        label = ((chip - core) % chips) ^ (1 << bit)
        pairs.append((m, 2 * ((label + core) % chips) + core))
    return pairs


def group_pairs(groups, members, bit):
    minor = GROUP_MINOR if groups % GROUP_MINOR == 0 else 1
    major = groups // minor

    def label(g, core):
        y, x = divmod(g, minor)
        return ((y - core) % major) * minor + (x - core) % minor

    def unlabel(l, core):
        y, x = divmod(l, minor)
        return ((y + core) % major) * minor + (x + core) % minor

    pairs = []
    for g in range(groups):
        for m in range(members):
            core = m % 2
            partner = unlabel(label(g, core) ^ (1 << bit), core)
            pairs.append((g * members + m, partner * members + m))
    return pairs


def halve(acc, bit):
    pairs = acc.reshape(acc.shape[0] // 2, 2, *acc.shape[1:])
    keep = lax.dynamic_index_in_dim(pairs, bit, 1, keepdims=False)
    send = lax.dynamic_index_in_dim(pairs, 1 - bit, 1, keepdims=False)
    return keep, send


def reduce_rows(part):
    members = lax.axis_size("member")
    groups = lax.axis_size("group")
    member_here = lax.axis_index("member")
    chips = members // 2
    chip, core = member_here // 2, member_here % 2
    rows, cols = part.shape
    acc = part.reshape(members, rows // members, cols)
    keep, send = halve(acc, core)
    sent = lax.ppermute(send.astype(jnp.bfloat16), "member", xor_pairs(members, 0))
    acc = keep + sent.astype(jnp.float32)
    acc = lax.dynamic_slice_in_dim(jnp.concatenate([acc, acc], axis=0), core, chips, 0)
    label = (chip - core) % chips
    for k in range(chips.bit_length() - 1):
        keep, send = halve(acc, (label >> k) & 1)
        sent = lax.ppermute(send.astype(jnp.bfloat16), "member", shifted_pairs(members, k))
        acc = keep + sent.astype(jnp.float32)
    acc = acc.reshape(rows // members, cols)
    for k in range(groups.bit_length() - 1):
        acc = acc + lax.ppermute(acc, ("group", "member"), group_pairs(groups, members, k))
    return acc


def on_device(feats, transform, bias, tile_list, nbr_slot, nbr_weight, cotangent):
    rows_dev, feat_width = feats.shape
    hidden_width = transform.shape[1]
    blocks, tiles_per = tile_list.shape
    block_rows = rows_dev // blocks
    members = lax.axis_size("member")
    groups = lax.axis_size("group")
    member_here = lax.axis_index("member")
    tiles_dev = rows_dev // TILE
    cand_width = tiles_per * TILE
    preact = jnp.dot(feats, transform, preferred_element_type=jnp.float32) + bias
    message = jnp.maximum(preact, 0.0).astype(jnp.bfloat16)
    own_tiles = message.reshape(tiles_dev, TILE, hidden_width)
    holder = tile_list // tiles_dev
    local_index = tile_list % tiles_dev
    foreign = holder != member_here
    peer_ids = lax.broadcasted_iota(jnp.int32, (1, 1, members), 2)
    matched = (holder[..., None] == peer_ids) & foreign[..., None]
    wanted = jnp.max(jnp.where(matched, local_index[..., None], -1), axis=(0, 1))
    asked_for = lax.all_to_all(
        wanted.reshape(members, 1), "member", split_axis=0, concat_axis=0, tiled=True
    )[:, 0]
    served = jnp.clip(asked_for, 0, tiles_dev - 1)
    remote = lax.all_to_all(own_tiles[served], "member", split_axis=0, concat_axis=0, tiled=True)
    pool_index = jnp.where(foreign, holder, members + local_index)
    pool_rows = (members + tiles_dev) * TILE
    slot_pool_row = (pool_index[:, :, None] * TILE + jnp.arange(TILE, dtype=jnp.int32)).reshape(
        blocks, cand_width
    )
    place = (
        slot_pool_row[:, :, None] == lax.broadcasted_iota(jnp.int32, (1, 1, pool_rows), 2)
    ).astype(jnp.bfloat16)
    slot_rows = nbr_slot.reshape(blocks, block_rows, -1)
    weights = nbr_weight.reshape(blocks, block_rows, -1)
    adjacency = adjacency_of(slot_rows, weights, cand_width)
    pool_adjacency = jnp.einsum(
        "brc,bcp->brp", adjacency, place, preferred_element_type=jnp.float32
    ).astype(jnp.bfloat16)
    remote_rows = members * TILE
    pool_adjacency = pool_adjacency.reshape(rows_dev, pool_rows)
    weight_total = jnp.sum(weights, axis=2).astype(jnp.float32)[..., None]
    gathered = jnp.dot(
        pool_adjacency[:, remote_rows:], message, preferred_element_type=jnp.float32
    ) + jnp.dot(
        pool_adjacency[:, :remote_rows],
        remote.reshape(remote_rows, hidden_width),
        preferred_element_type=jnp.float32,
    )
    combined = gathered.reshape(blocks, block_rows, hidden_width) / weight_total + message.reshape(
        blocks, block_rows, hidden_width
    ).astype(jnp.float32)
    inv_rms = lax.rsqrt(jnp.mean(combined * combined, axis=2, keepdims=True) + 1e-06)
    normed = combined * inv_rms
    embedding = normed.astype(jnp.bfloat16).reshape(rows_dev, hidden_width)
    incoming = cotangent.reshape(blocks, block_rows, hidden_width).astype(jnp.float32)
    mixed_grad = inv_rms * (incoming - normed * jnp.mean(incoming * normed, axis=2, keepdims=True))
    agg_grad = (mixed_grad / weight_total).astype(jnp.bfloat16).reshape(rows_dev, hidden_width)
    by_rows = (((0,), (0,)), ((), ()))
    remote_grad = lax.dot_general(
        pool_adjacency[:, :remote_rows], agg_grad, by_rows, preferred_element_type=jnp.float32
    )
    returned = remote_grad.astype(jnp.bfloat16).reshape(members, TILE, hidden_width)
    came_back = lax.all_to_all(returned, "member", split_axis=0, concat_axis=0, tiled=True)
    own_grad = lax.dot_general(
        pool_adjacency[:, remote_rows:], agg_grad, by_rows, preferred_element_type=jnp.float32
    )
    back_to = (
        (served[:, None] == lax.broadcasted_iota(jnp.int32, (1, tiles_dev), 1))
        & (asked_for >= 0)[:, None]
    ).astype(jnp.bfloat16)
    tile_grad = own_grad.reshape(tiles_dev, TILE * hidden_width) + lax.dot_general(
        back_to,
        came_back.reshape(members, TILE * hidden_width),
        by_rows,
        preferred_element_type=jnp.float32,
    )
    message_grad = mixed_grad.reshape(rows_dev, hidden_width) + tile_grad.reshape(
        rows_dev, hidden_width
    )
    pre_grad = jnp.where(preact > 0, message_grad, 0.0).astype(jnp.bfloat16)
    feat_grad = lax.dot_general(
        pre_grad, transform, (((1,), (1,)), ((), ())), preferred_element_type=jnp.float32
    ).astype(jnp.bfloat16)
    partial = lax.dot_general(
        feats, pre_grad, (((0,), (0,)), ((), ())), preferred_element_type=jnp.float32
    )
    factor = 1.0 / math.sqrt(rows_dev * members * groups)
    transform_grad = reduce_rows(partial) * factor
    return (embedding, feat_grad, transform_grad)


def solution(mesh):
    return jax.shard_map(
        on_device,
        mesh=mesh,
        in_specs=(
            P(("group", "member"), None),
            P(),
            P(),
            P(("group", "member"), None),
            P(("group", "member"), None),
            P(("group", "member"), None),
            P(("group", "member"), None),
        ),
        out_specs=(P(("group", "member"), None), P(("group", "member"), None), P("member", None)),
        check_vma=False,
    )
```

```python
import math

import jax
import jax.numpy as jnp
from jax import lax
from jax.sharding import PartitionSpec as P

TILE = 32


def adjacency_of(slot_rows, weights, cand_width):
    columns = lax.broadcasted_iota(jnp.int32, slot_rows.shape + (cand_width,), slot_rows.ndim)
    matched_weights = jnp.where(slot_rows[..., None] == columns, weights[..., None], 0)
    return jnp.sum(matched_weights, axis=-2).astype(jnp.bfloat16)


def xor_pairs(n, bit):
    return [(i, i ^ (1 << bit)) for i in range(n)]


def shifted_pairs(members, bit):
    chips = members // 2
    pairs = []
    for m in range(members):
        chip, core = divmod(m, 2)
        label = ((chip - core) % chips) ^ (1 << bit)
        pairs.append((m, 2 * ((label + core) % chips) + core))
    return pairs


def halve(acc, bit):
    pairs = acc.reshape(acc.shape[0] // 2, 2, *acc.shape[1:])
    keep = lax.dynamic_index_in_dim(pairs, bit, 1, keepdims=False)
    send = lax.dynamic_index_in_dim(pairs, 1 - bit, 1, keepdims=False)
    return keep, send


def reduce_rows(part):
    members = lax.axis_size("member")
    groups = lax.axis_size("group")
    member_here = lax.axis_index("member")
    chips = members // 2
    chip, core = member_here // 2, member_here % 2
    rows, cols = part.shape
    acc = part.reshape(members, rows // members, cols)
    keep, send = halve(acc, core)
    sent = lax.ppermute(send.astype(jnp.bfloat16), "member", xor_pairs(members, 0))
    acc = keep + sent.astype(jnp.float32)
    acc = lax.dynamic_slice_in_dim(jnp.concatenate([acc, acc], axis=0), core, chips, 0)
    label = (chip - core) % chips
    for k in range(chips.bit_length() - 1):
        keep, send = halve(acc, (label >> k) & 1)
        sent = lax.ppermute(send.astype(jnp.bfloat16), "member", shifted_pairs(members, k))
        acc = keep + sent.astype(jnp.float32)
    slices = acc.reshape(groups, -1)
    mine = jnp.sum(lax.all_to_all(slices, "group", split_axis=0, concat_axis=0, tiled=True), axis=0)
    every = lax.all_to_all(
        jnp.broadcast_to(mine, slices.shape), "group", split_axis=0, concat_axis=0, tiled=True
    )
    return every.reshape(rows // members, cols)


def on_device(feats, transform, bias, tile_list, nbr_slot, nbr_weight, cotangent):
    rows_dev, feat_width = feats.shape
    hidden_width = transform.shape[1]
    blocks, tiles_per = tile_list.shape
    block_rows = rows_dev // blocks
    members = lax.axis_size("member")
    groups = lax.axis_size("group")
    member_here = lax.axis_index("member")
    tiles_dev = rows_dev // TILE
    cand_width = tiles_per * TILE
    preact = jnp.dot(feats, transform, preferred_element_type=jnp.float32) + bias
    message = jnp.maximum(preact, 0.0).astype(jnp.bfloat16)
    own_tiles = message.reshape(tiles_dev, TILE, hidden_width)
    holder = tile_list // tiles_dev
    local_index = tile_list % tiles_dev
    foreign = holder != member_here
    peer_ids = lax.broadcasted_iota(jnp.int32, (1, 1, members), 2)
    matched = (holder[..., None] == peer_ids) & foreign[..., None]
    wanted = jnp.max(jnp.where(matched, local_index[..., None], -1), axis=(0, 1))
    asked_for = lax.all_to_all(
        wanted.reshape(members, 1), "member", split_axis=0, concat_axis=0, tiled=True
    )[:, 0]
    served = jnp.clip(asked_for, 0, tiles_dev - 1)
    remote = lax.all_to_all(own_tiles[served], "member", split_axis=0, concat_axis=0, tiled=True)
    pool_index = jnp.where(foreign, holder, members + local_index)
    pool_rows = (members + tiles_dev) * TILE
    slot_pool_row = (pool_index[:, :, None] * TILE + jnp.arange(TILE, dtype=jnp.int32)).reshape(
        blocks, cand_width
    )
    place = (
        slot_pool_row[:, :, None] == lax.broadcasted_iota(jnp.int32, (1, 1, pool_rows), 2)
    ).astype(jnp.bfloat16)
    slot_rows = nbr_slot.reshape(blocks, block_rows, -1)
    weights = nbr_weight.reshape(blocks, block_rows, -1)
    adjacency = adjacency_of(slot_rows, weights, cand_width)
    pool_adjacency = jnp.einsum(
        "brc,bcp->brp", adjacency, place, preferred_element_type=jnp.float32
    ).astype(jnp.bfloat16)
    remote_rows = members * TILE
    pool_adjacency = pool_adjacency.reshape(rows_dev, pool_rows)
    weight_total = jnp.sum(weights, axis=2).astype(jnp.float32)[..., None]
    gathered = jnp.dot(
        pool_adjacency[:, remote_rows:], message, preferred_element_type=jnp.float32
    ) + jnp.dot(
        pool_adjacency[:, :remote_rows],
        remote.reshape(remote_rows, hidden_width),
        preferred_element_type=jnp.float32,
    )
    combined = gathered.reshape(blocks, block_rows, hidden_width) / weight_total + message.reshape(
        blocks, block_rows, hidden_width
    ).astype(jnp.float32)
    inv_rms = lax.rsqrt(jnp.mean(combined * combined, axis=2, keepdims=True) + 1e-06)
    normed = combined * inv_rms
    embedding = normed.astype(jnp.bfloat16).reshape(rows_dev, hidden_width)
    incoming = cotangent.reshape(blocks, block_rows, hidden_width).astype(jnp.float32)
    mixed_grad = inv_rms * (incoming - normed * jnp.mean(incoming * normed, axis=2, keepdims=True))
    agg_grad = (mixed_grad / weight_total).astype(jnp.bfloat16).reshape(rows_dev, hidden_width)
    by_rows = (((0,), (0,)), ((), ()))
    remote_grad = lax.dot_general(
        pool_adjacency[:, :remote_rows], agg_grad, by_rows, preferred_element_type=jnp.float32
    )
    returned = remote_grad.astype(jnp.bfloat16).reshape(members, TILE, hidden_width)
    came_back = lax.all_to_all(returned, "member", split_axis=0, concat_axis=0, tiled=True)
    own_grad = lax.dot_general(
        pool_adjacency[:, remote_rows:], agg_grad, by_rows, preferred_element_type=jnp.float32
    )
    back_to = (
        (served[:, None] == lax.broadcasted_iota(jnp.int32, (1, tiles_dev), 1))
        & (asked_for >= 0)[:, None]
    ).astype(jnp.bfloat16)
    tile_grad = own_grad.reshape(tiles_dev, TILE * hidden_width) + lax.dot_general(
        back_to,
        came_back.reshape(members, TILE * hidden_width),
        by_rows,
        preferred_element_type=jnp.float32,
    )
    message_grad = mixed_grad.reshape(rows_dev, hidden_width) + tile_grad.reshape(
        rows_dev, hidden_width
    )
    pre_grad = jnp.where(preact > 0, message_grad, 0.0).astype(jnp.bfloat16)
    feat_grad = lax.dot_general(
        pre_grad, transform, (((1,), (1,)), ((), ())), preferred_element_type=jnp.float32
    ).astype(jnp.bfloat16)
    partial = lax.dot_general(
        feats, pre_grad, (((0,), (0,)), ((), ())), preferred_element_type=jnp.float32
    )
    factor = 1.0 / math.sqrt(rows_dev * members * groups)
    transform_grad = reduce_rows(partial) * factor
    return (embedding, feat_grad, transform_grad)


def solution(mesh):
    return jax.shard_map(
        on_device,
        mesh=mesh,
        in_specs=(
            P(("group", "member"), None),
            P(),
            P(),
            P(("group", "member"), None),
            P(("group", "member"), None),
            P(("group", "member"), None),
            P(("group", "member"), None),
        ),
        out_specs=(P(("group", "member"), None), P(("group", "member"), None), P("member", None)),
        check_vma=False,
    )
```

```python
import math

import jax
import jax.numpy as jnp
from jax import lax
from jax.sharding import PartitionSpec as P

TILE = 32


def adjacency_of(slot_rows, weights, cand_width):
    columns = lax.broadcasted_iota(jnp.int32, slot_rows.shape + (cand_width,), slot_rows.ndim)
    matched_weights = jnp.where(slot_rows[..., None] == columns, weights[..., None], 0)
    return jnp.sum(matched_weights, axis=-2).astype(jnp.bfloat16)


def xor_pairs(n, bit):
    return [(i, i ^ (1 << bit)) for i in range(n)]


def reduce_rows(part):
    members = lax.axis_size("member")
    groups = lax.axis_size("group")
    core = lax.axis_index("member") % 2
    rows, cols = part.shape
    halves = part.reshape(rows, 2, cols // 2)
    keep = lax.dynamic_index_in_dim(halves, core, 1, keepdims=False)
    send = lax.dynamic_index_in_dim(halves, 1 - core, 1, keepdims=False)
    pair_sum = keep + lax.ppermute(send.astype(jnp.bfloat16), "member", xor_pairs(members, 0)).astype(
        jnp.float32
    )
    to_members = pair_sum.astype(jnp.bfloat16).reshape(members, rows // members, cols // 2)
    from_members = lax.all_to_all(to_members, "member", split_axis=0, concat_axis=0, tiled=True)
    by_half = jnp.sum(
        from_members.astype(jnp.float32).reshape(members // 2, 2, rows // members, cols // 2), axis=0
    )
    acc = jnp.transpose(by_half, (1, 0, 2)).reshape(rows // members, cols)
    slices = acc.reshape(groups, -1)
    mine = jnp.sum(lax.all_to_all(slices, "group", split_axis=0, concat_axis=0, tiled=True), axis=0)
    every = lax.all_to_all(
        jnp.broadcast_to(mine, slices.shape), "group", split_axis=0, concat_axis=0, tiled=True
    )
    return every.reshape(rows // members, cols)


def on_device(feats, transform, bias, tile_list, nbr_slot, nbr_weight, cotangent):
    rows_dev, feat_width = feats.shape
    hidden_width = transform.shape[1]
    blocks, tiles_per = tile_list.shape
    block_rows = rows_dev // blocks
    members = lax.axis_size("member")
    groups = lax.axis_size("group")
    member_here = lax.axis_index("member")
    tiles_dev = rows_dev // TILE
    cand_width = tiles_per * TILE
    preact = jnp.dot(feats, transform, preferred_element_type=jnp.float32) + bias
    message = jnp.maximum(preact, 0.0).astype(jnp.bfloat16)
    own_tiles = message.reshape(tiles_dev, TILE, hidden_width)
    holder = tile_list // tiles_dev
    local_index = tile_list % tiles_dev
    foreign = holder != member_here
    peer_ids = lax.broadcasted_iota(jnp.int32, (1, 1, members), 2)
    matched = (holder[..., None] == peer_ids) & foreign[..., None]
    wanted = jnp.max(jnp.where(matched, local_index[..., None], -1), axis=(0, 1))
    asked_for = lax.all_to_all(
        wanted.reshape(members, 1), "member", split_axis=0, concat_axis=0, tiled=True
    )[:, 0]
    served = jnp.clip(asked_for, 0, tiles_dev - 1)
    remote = lax.all_to_all(own_tiles[served], "member", split_axis=0, concat_axis=0, tiled=True)
    pool_index = jnp.where(foreign, holder, members + local_index)
    pool_rows = (members + tiles_dev) * TILE
    slot_pool_row = (pool_index[:, :, None] * TILE + jnp.arange(TILE, dtype=jnp.int32)).reshape(
        blocks, cand_width
    )
    place = (
        slot_pool_row[:, :, None] == lax.broadcasted_iota(jnp.int32, (1, 1, pool_rows), 2)
    ).astype(jnp.bfloat16)
    slot_rows = nbr_slot.reshape(blocks, block_rows, -1)
    weights = nbr_weight.reshape(blocks, block_rows, -1)
    adjacency = adjacency_of(slot_rows, weights, cand_width)
    pool_adjacency = jnp.einsum(
        "brc,bcp->brp", adjacency, place, preferred_element_type=jnp.float32
    ).astype(jnp.bfloat16)
    remote_rows = members * TILE
    pool_adjacency = pool_adjacency.reshape(rows_dev, pool_rows)
    weight_total = jnp.sum(weights, axis=2).astype(jnp.float32)[..., None]
    gathered = jnp.dot(
        pool_adjacency[:, remote_rows:], message, preferred_element_type=jnp.float32
    ) + jnp.dot(
        pool_adjacency[:, :remote_rows],
        remote.reshape(remote_rows, hidden_width),
        preferred_element_type=jnp.float32,
    )
    combined = gathered.reshape(blocks, block_rows, hidden_width) / weight_total + message.reshape(
        blocks, block_rows, hidden_width
    ).astype(jnp.float32)
    inv_rms = lax.rsqrt(jnp.mean(combined * combined, axis=2, keepdims=True) + 1e-06)
    normed = combined * inv_rms
    embedding = normed.astype(jnp.bfloat16).reshape(rows_dev, hidden_width)
    incoming = cotangent.reshape(blocks, block_rows, hidden_width).astype(jnp.float32)
    mixed_grad = inv_rms * (incoming - normed * jnp.mean(incoming * normed, axis=2, keepdims=True))
    agg_grad = (mixed_grad / weight_total).astype(jnp.bfloat16).reshape(rows_dev, hidden_width)
    by_rows = (((0,), (0,)), ((), ()))
    remote_grad = lax.dot_general(
        pool_adjacency[:, :remote_rows], agg_grad, by_rows, preferred_element_type=jnp.float32
    )
    returned = remote_grad.astype(jnp.bfloat16).reshape(members, TILE, hidden_width)
    came_back = lax.all_to_all(returned, "member", split_axis=0, concat_axis=0, tiled=True)
    own_grad = lax.dot_general(
        pool_adjacency[:, remote_rows:], agg_grad, by_rows, preferred_element_type=jnp.float32
    )
    back_to = (
        (served[:, None] == lax.broadcasted_iota(jnp.int32, (1, tiles_dev), 1))
        & (asked_for >= 0)[:, None]
    ).astype(jnp.bfloat16)
    tile_grad = own_grad.reshape(tiles_dev, TILE * hidden_width) + lax.dot_general(
        back_to,
        came_back.reshape(members, TILE * hidden_width),
        by_rows,
        preferred_element_type=jnp.float32,
    )
    message_grad = mixed_grad.reshape(rows_dev, hidden_width) + tile_grad.reshape(
        rows_dev, hidden_width
    )
    pre_grad = jnp.where(preact > 0, message_grad, 0.0).astype(jnp.bfloat16)
    feat_grad = lax.dot_general(
        pre_grad, transform, (((1,), (1,)), ((), ())), preferred_element_type=jnp.float32
    ).astype(jnp.bfloat16)
    partial = lax.dot_general(
        feats, pre_grad, (((0,), (0,)), ((), ())), preferred_element_type=jnp.float32
    )
    factor = 1.0 / math.sqrt(rows_dev * members * groups)
    transform_grad = reduce_rows(partial) * factor
    return (embedding, feat_grad, transform_grad)


def solution(mesh):
    return jax.shard_map(
        on_device,
        mesh=mesh,
        in_specs=(
            P(("group", "member"), None),
            P(),
            P(),
            P(("group", "member"), None),
            P(("group", "member"), None),
            P(("group", "member"), None),
            P(("group", "member"), None),
        ),
        out_specs=(P(("group", "member"), None), P(("group", "member"), None), P("member", None)),
        check_vma=False,
    )
```

```python
import math

import jax
import jax.numpy as jnp
from jax import lax
from jax.sharding import PartitionSpec as P

TILE = 32


def adjacency_of(slot_rows, weights, cand_width):
    columns = lax.broadcasted_iota(jnp.int32, slot_rows.shape + (cand_width,), slot_rows.ndim)
    matched_weights = jnp.where(slot_rows[..., None] == columns, weights[..., None], 0)
    return jnp.sum(matched_weights, axis=-2).astype(jnp.bfloat16)


def xor_pairs(n, bit):
    return [(i, i ^ (1 << bit)) for i in range(n)]


def reduce_rows(part):
    members = lax.axis_size("member")
    groups = lax.axis_size("group")
    core = lax.axis_index("member") % 2
    rows, cols = part.shape
    halves = part.reshape(rows, 2, cols // 2)
    keep = lax.dynamic_index_in_dim(halves, core, 1, keepdims=False)
    send = lax.dynamic_index_in_dim(halves, 1 - core, 1, keepdims=False)
    pair_sum = keep + lax.ppermute(send.astype(jnp.bfloat16), "member", xor_pairs(members, 0)).astype(
        jnp.float32
    )
    block = rows // members
    share = block // groups
    chunks = pair_sum.astype(jnp.bfloat16).reshape(members, groups, share, cols // 2)
    chunks = jnp.transpose(chunks, (1, 0, 2, 3)).reshape(groups * members, share, cols // 2)
    got = lax.all_to_all(chunks, ("group", "member"), split_axis=0, concat_axis=0, tiled=True)
    by_half = jnp.sum(
        got.astype(jnp.float32).reshape(groups * members // 2, 2, share, cols // 2), axis=0
    )
    mine = jnp.transpose(by_half, (1, 0, 2)).reshape(share * cols)
    every = lax.all_to_all(
        jnp.broadcast_to(mine, (groups, share * cols)), "group", split_axis=0, concat_axis=0, tiled=True
    )
    return every.reshape(rows // members, cols)


def on_device(feats, transform, bias, tile_list, nbr_slot, nbr_weight, cotangent):
    rows_dev, feat_width = feats.shape
    hidden_width = transform.shape[1]
    blocks, tiles_per = tile_list.shape
    block_rows = rows_dev // blocks
    members = lax.axis_size("member")
    groups = lax.axis_size("group")
    member_here = lax.axis_index("member")
    tiles_dev = rows_dev // TILE
    cand_width = tiles_per * TILE
    preact = jnp.dot(feats, transform, preferred_element_type=jnp.float32) + bias
    message = jnp.maximum(preact, 0.0).astype(jnp.bfloat16)
    own_tiles = message.reshape(tiles_dev, TILE, hidden_width)
    holder = tile_list // tiles_dev
    local_index = tile_list % tiles_dev
    foreign = holder != member_here
    peer_ids = lax.broadcasted_iota(jnp.int32, (1, 1, members), 2)
    matched = (holder[..., None] == peer_ids) & foreign[..., None]
    wanted = jnp.max(jnp.where(matched, local_index[..., None], -1), axis=(0, 1))
    asked_for = lax.all_to_all(
        wanted.reshape(members, 1), "member", split_axis=0, concat_axis=0, tiled=True
    )[:, 0]
    served = jnp.clip(asked_for, 0, tiles_dev - 1)
    remote = lax.all_to_all(own_tiles[served], "member", split_axis=0, concat_axis=0, tiled=True)
    pool_index = jnp.where(foreign, holder, members + local_index)
    pool_rows = (members + tiles_dev) * TILE
    slot_pool_row = (pool_index[:, :, None] * TILE + jnp.arange(TILE, dtype=jnp.int32)).reshape(
        blocks, cand_width
    )
    place = (
        slot_pool_row[:, :, None] == lax.broadcasted_iota(jnp.int32, (1, 1, pool_rows), 2)
    ).astype(jnp.bfloat16)
    slot_rows = nbr_slot.reshape(blocks, block_rows, -1)
    weights = nbr_weight.reshape(blocks, block_rows, -1)
    adjacency = adjacency_of(slot_rows, weights, cand_width)
    pool_adjacency = jnp.einsum(
        "brc,bcp->brp", adjacency, place, preferred_element_type=jnp.float32
    ).astype(jnp.bfloat16)
    remote_rows = members * TILE
    pool_adjacency = pool_adjacency.reshape(rows_dev, pool_rows)
    weight_total = jnp.sum(weights, axis=2).astype(jnp.float32)[..., None]
    gathered = jnp.dot(
        pool_adjacency[:, remote_rows:], message, preferred_element_type=jnp.float32
    ) + jnp.dot(
        pool_adjacency[:, :remote_rows],
        remote.reshape(remote_rows, hidden_width),
        preferred_element_type=jnp.float32,
    )
    combined = gathered.reshape(blocks, block_rows, hidden_width) / weight_total + message.reshape(
        blocks, block_rows, hidden_width
    ).astype(jnp.float32)
    inv_rms = lax.rsqrt(jnp.mean(combined * combined, axis=2, keepdims=True) + 1e-06)
    normed = combined * inv_rms
    embedding = normed.astype(jnp.bfloat16).reshape(rows_dev, hidden_width)
    incoming = cotangent.reshape(blocks, block_rows, hidden_width).astype(jnp.float32)
    mixed_grad = inv_rms * (incoming - normed * jnp.mean(incoming * normed, axis=2, keepdims=True))
    agg_grad = (mixed_grad / weight_total).astype(jnp.bfloat16).reshape(rows_dev, hidden_width)
    by_rows = (((0,), (0,)), ((), ()))
    remote_grad = lax.dot_general(
        pool_adjacency[:, :remote_rows], agg_grad, by_rows, preferred_element_type=jnp.float32
    )
    returned = remote_grad.astype(jnp.bfloat16).reshape(members, TILE, hidden_width)
    came_back = lax.all_to_all(returned, "member", split_axis=0, concat_axis=0, tiled=True)
    own_grad = lax.dot_general(
        pool_adjacency[:, remote_rows:], agg_grad, by_rows, preferred_element_type=jnp.float32
    )
    back_to = (
        (served[:, None] == lax.broadcasted_iota(jnp.int32, (1, tiles_dev), 1))
        & (asked_for >= 0)[:, None]
    ).astype(jnp.bfloat16)
    tile_grad = own_grad.reshape(tiles_dev, TILE * hidden_width) + lax.dot_general(
        back_to,
        came_back.reshape(members, TILE * hidden_width),
        by_rows,
        preferred_element_type=jnp.float32,
    )
    message_grad = mixed_grad.reshape(rows_dev, hidden_width) + tile_grad.reshape(
        rows_dev, hidden_width
    )
    pre_grad = jnp.where(preact > 0, message_grad, 0.0).astype(jnp.bfloat16)
    feat_grad = lax.dot_general(
        pre_grad, transform, (((1,), (1,)), ((), ())), preferred_element_type=jnp.float32
    ).astype(jnp.bfloat16)
    partial = lax.dot_general(
        feats, pre_grad, (((0,), (0,)), ((), ())), preferred_element_type=jnp.float32
    )
    factor = 1.0 / math.sqrt(rows_dev * members * groups)
    transform_grad = reduce_rows(partial) * factor
    return (embedding, feat_grad, transform_grad)


def solution(mesh):
    return jax.shard_map(
        on_device,
        mesh=mesh,
        in_specs=(
            P(("group", "member"), None),
            P(),
            P(),
            P(("group", "member"), None),
            P(("group", "member"), None),
            P(("group", "member"), None),
            P(("group", "member"), None),
        ),
        out_specs=(P(("group", "member"), None), P(("group", "member"), None), P("member", None)),
        check_vma=False,
    )
```

```python
import math

import jax
import jax.numpy as jnp
from jax import lax
from jax.sharding import PartitionSpec as P

TILE = 32


def adjacency_of(slot_rows, weights, cand_width):
    columns = lax.broadcasted_iota(jnp.int32, slot_rows.shape + (cand_width,), slot_rows.ndim)
    matched_weights = jnp.where(slot_rows[..., None] == columns, weights[..., None], 0)
    return jnp.sum(matched_weights, axis=-2).astype(jnp.bfloat16)


def xor_pairs(n, bit):
    return [(i, i ^ (1 << bit)) for i in range(n)]


def reduce_rows(part):
    members = lax.axis_size("member")
    groups = lax.axis_size("group")
    core = lax.axis_index("member") % 2
    rows, cols = part.shape
    left, right = part[:, : cols // 2], part[:, cols // 2 :]
    keep = jnp.where(core == 0, left, right)
    send = jnp.where(core == 0, right, left)
    pair_sum = keep + lax.ppermute(send.astype(jnp.bfloat16), "member", xor_pairs(members, 0)).astype(
        jnp.float32
    )
    block = rows // members
    share = block // groups
    chunks = pair_sum.astype(jnp.bfloat16).reshape(members, groups, share, cols // 2)
    chunks = jnp.transpose(chunks, (1, 0, 2, 3)).reshape(groups * members, share, cols // 2)
    got = lax.all_to_all(chunks, ("group", "member"), split_axis=0, concat_axis=0, tiled=True)
    by_half = jnp.sum(
        got.astype(jnp.float32).reshape(groups * members // 2, 2, share, cols // 2), axis=0
    )
    mine = jnp.transpose(by_half, (1, 0, 2)).reshape(share * cols)
    every = lax.all_to_all(
        jnp.broadcast_to(mine, (groups, share * cols)), "group", split_axis=0, concat_axis=0, tiled=True
    )
    return every.reshape(rows // members, cols)


def on_device(feats, transform, bias, tile_list, nbr_slot, nbr_weight, cotangent):
    rows_dev, feat_width = feats.shape
    hidden_width = transform.shape[1]
    blocks, tiles_per = tile_list.shape
    block_rows = rows_dev // blocks
    members = lax.axis_size("member")
    groups = lax.axis_size("group")
    member_here = lax.axis_index("member")
    tiles_dev = rows_dev // TILE
    cand_width = tiles_per * TILE
    preact = jnp.dot(feats, transform, preferred_element_type=jnp.float32) + bias
    message = jnp.maximum(preact, 0.0).astype(jnp.bfloat16)
    own_tiles = message.reshape(tiles_dev, TILE, hidden_width)
    holder = tile_list // tiles_dev
    local_index = tile_list % tiles_dev
    foreign = holder != member_here
    peer_ids = lax.broadcasted_iota(jnp.int32, (1, 1, members), 2)
    matched = (holder[..., None] == peer_ids) & foreign[..., None]
    wanted = jnp.max(jnp.where(matched, local_index[..., None], -1), axis=(0, 1))
    asked_for = lax.all_to_all(
        wanted.reshape(members, 1), "member", split_axis=0, concat_axis=0, tiled=True
    )[:, 0]
    served = jnp.clip(asked_for, 0, tiles_dev - 1)
    remote = lax.all_to_all(own_tiles[served], "member", split_axis=0, concat_axis=0, tiled=True)
    pool_index = jnp.where(foreign, holder, members + local_index)
    pool_rows = (members + tiles_dev) * TILE
    slot_pool_row = (pool_index[:, :, None] * TILE + jnp.arange(TILE, dtype=jnp.int32)).reshape(
        blocks, cand_width
    )
    place = (
        slot_pool_row[:, :, None] == lax.broadcasted_iota(jnp.int32, (1, 1, pool_rows), 2)
    ).astype(jnp.bfloat16)
    slot_rows = nbr_slot.reshape(blocks, block_rows, -1)
    weights = nbr_weight.reshape(blocks, block_rows, -1)
    adjacency = adjacency_of(slot_rows, weights, cand_width)
    pool_adjacency = jnp.einsum(
        "brc,bcp->brp", adjacency, place, preferred_element_type=jnp.float32
    ).astype(jnp.bfloat16)
    remote_rows = members * TILE
    pool_adjacency = pool_adjacency.reshape(rows_dev, pool_rows)
    weight_total = jnp.sum(weights, axis=2).astype(jnp.float32)[..., None]
    gathered = jnp.dot(
        pool_adjacency[:, remote_rows:], message, preferred_element_type=jnp.float32
    ) + jnp.dot(
        pool_adjacency[:, :remote_rows],
        remote.reshape(remote_rows, hidden_width),
        preferred_element_type=jnp.float32,
    )
    combined = gathered.reshape(blocks, block_rows, hidden_width) / weight_total + message.reshape(
        blocks, block_rows, hidden_width
    ).astype(jnp.float32)
    inv_rms = lax.rsqrt(jnp.mean(combined * combined, axis=2, keepdims=True) + 1e-06)
    normed = combined * inv_rms
    embedding = normed.astype(jnp.bfloat16).reshape(rows_dev, hidden_width)
    incoming = cotangent.reshape(blocks, block_rows, hidden_width).astype(jnp.float32)
    mixed_grad = inv_rms * (incoming - normed * jnp.mean(incoming * normed, axis=2, keepdims=True))
    agg_grad = (mixed_grad / weight_total).astype(jnp.bfloat16).reshape(rows_dev, hidden_width)
    by_rows = (((0,), (0,)), ((), ()))
    remote_grad = lax.dot_general(
        pool_adjacency[:, :remote_rows], agg_grad, by_rows, preferred_element_type=jnp.float32
    )
    returned = remote_grad.astype(jnp.bfloat16).reshape(members, TILE, hidden_width)
    came_back = lax.all_to_all(returned, "member", split_axis=0, concat_axis=0, tiled=True)
    own_grad = lax.dot_general(
        pool_adjacency[:, remote_rows:], agg_grad, by_rows, preferred_element_type=jnp.float32
    )
    back_to = (
        (served[:, None] == lax.broadcasted_iota(jnp.int32, (1, tiles_dev), 1))
        & (asked_for >= 0)[:, None]
    ).astype(jnp.bfloat16)
    tile_grad = own_grad.reshape(tiles_dev, TILE * hidden_width) + lax.dot_general(
        back_to,
        came_back.reshape(members, TILE * hidden_width),
        by_rows,
        preferred_element_type=jnp.float32,
    )
    message_grad = mixed_grad.reshape(rows_dev, hidden_width) + tile_grad.reshape(
        rows_dev, hidden_width
    )
    pre_grad = jnp.where(preact > 0, message_grad, 0.0).astype(jnp.bfloat16)
    feat_grad = lax.dot_general(
        pre_grad, transform, (((1,), (1,)), ((), ())), preferred_element_type=jnp.float32
    ).astype(jnp.bfloat16)
    partial = lax.dot_general(
        feats, pre_grad, (((0,), (0,)), ((), ())), preferred_element_type=jnp.float32
    )
    factor = 1.0 / math.sqrt(rows_dev * members * groups)
    transform_grad = reduce_rows(partial) * factor
    return (embedding, feat_grad, transform_grad)


def solution(mesh):
    return jax.shard_map(
        on_device,
        mesh=mesh,
        in_specs=(
            P(("group", "member"), None),
            P(),
            P(),
            P(("group", "member"), None),
            P(("group", "member"), None),
            P(("group", "member"), None),
            P(("group", "member"), None),
        ),
        out_specs=(P(("group", "member"), None), P(("group", "member"), None), P("member", None)),
        check_vma=False,
    )
```

```python
import math

import jax
import jax.numpy as jnp
from jax import lax
from jax.sharding import PartitionSpec as P

TILE = 32


def adjacency_of(slot_rows, weights, cand_width):
    columns = lax.broadcasted_iota(jnp.int32, slot_rows.shape + (cand_width,), slot_rows.ndim)
    matched_weights = jnp.where(slot_rows[..., None] == columns, weights[..., None], 0)
    return jnp.sum(matched_weights, axis=-2).astype(jnp.bfloat16)


def xor_pairs(n, bit):
    return [(i, i ^ (1 << bit)) for i in range(n)]


def reduce_rows(part):
    members = lax.axis_size("member")
    groups = lax.axis_size("group")
    core = lax.axis_index("member") % 2
    rows, cols = part.shape
    block = rows // members
    share = block // groups

    def chunk_order(x):
        x = x.reshape(members, groups, share, cols // 2)
        return jnp.transpose(x, (1, 0, 2, 3)).reshape(groups * members, share, cols // 2)

    left, right = part[:, : cols // 2], part[:, cols // 2 :]
    keep = chunk_order(jnp.where(core == 0, left, right))
    send = chunk_order(jnp.where(core == 0, right, left))
    pair_sum = keep + lax.ppermute(send.astype(jnp.bfloat16), "member", xor_pairs(members, 0)).astype(
        jnp.float32
    )
    got = lax.all_to_all(
        pair_sum.astype(jnp.bfloat16), ("group", "member"), split_axis=0, concat_axis=0, tiled=True
    )
    by_half = jnp.sum(
        got.astype(jnp.float32).reshape(groups * members // 2, 2, share, cols // 2), axis=0
    )
    mine = jnp.transpose(by_half, (1, 0, 2)).reshape(share * cols)
    every = lax.all_to_all(
        jnp.broadcast_to(mine, (groups, share * cols)), "group", split_axis=0, concat_axis=0, tiled=True
    )
    return every.reshape(rows // members, cols)


def on_device(feats, transform, bias, tile_list, nbr_slot, nbr_weight, cotangent):
    rows_dev, feat_width = feats.shape
    hidden_width = transform.shape[1]
    blocks, tiles_per = tile_list.shape
    block_rows = rows_dev // blocks
    members = lax.axis_size("member")
    groups = lax.axis_size("group")
    member_here = lax.axis_index("member")
    tiles_dev = rows_dev // TILE
    cand_width = tiles_per * TILE
    preact = jnp.dot(feats, transform, preferred_element_type=jnp.float32) + bias
    message = jnp.maximum(preact, 0.0).astype(jnp.bfloat16)
    own_tiles = message.reshape(tiles_dev, TILE, hidden_width)
    holder = tile_list // tiles_dev
    local_index = tile_list % tiles_dev
    foreign = holder != member_here
    peer_ids = lax.broadcasted_iota(jnp.int32, (1, 1, members), 2)
    matched = (holder[..., None] == peer_ids) & foreign[..., None]
    wanted = jnp.max(jnp.where(matched, local_index[..., None], -1), axis=(0, 1))
    asked_for = lax.all_to_all(
        wanted.reshape(members, 1), "member", split_axis=0, concat_axis=0, tiled=True
    )[:, 0]
    served = jnp.clip(asked_for, 0, tiles_dev - 1)
    remote = lax.all_to_all(own_tiles[served], "member", split_axis=0, concat_axis=0, tiled=True)
    pool_index = jnp.where(foreign, holder, members + local_index)
    pool_rows = (members + tiles_dev) * TILE
    slot_pool_row = (pool_index[:, :, None] * TILE + jnp.arange(TILE, dtype=jnp.int32)).reshape(
        blocks, cand_width
    )
    place = (
        slot_pool_row[:, :, None] == lax.broadcasted_iota(jnp.int32, (1, 1, pool_rows), 2)
    ).astype(jnp.bfloat16)
    slot_rows = nbr_slot.reshape(blocks, block_rows, -1)
    weights = nbr_weight.reshape(blocks, block_rows, -1)
    adjacency = adjacency_of(slot_rows, weights, cand_width)
    pool_adjacency = jnp.einsum(
        "brc,bcp->brp", adjacency, place, preferred_element_type=jnp.float32
    ).astype(jnp.bfloat16)
    remote_rows = members * TILE
    pool_adjacency = pool_adjacency.reshape(rows_dev, pool_rows)
    weight_total = jnp.sum(weights, axis=2).astype(jnp.float32)[..., None]
    gathered = jnp.dot(
        pool_adjacency[:, remote_rows:], message, preferred_element_type=jnp.float32
    ) + jnp.dot(
        pool_adjacency[:, :remote_rows],
        remote.reshape(remote_rows, hidden_width),
        preferred_element_type=jnp.float32,
    )
    combined = gathered.reshape(blocks, block_rows, hidden_width) / weight_total + message.reshape(
        blocks, block_rows, hidden_width
    ).astype(jnp.float32)
    inv_rms = lax.rsqrt(jnp.mean(combined * combined, axis=2, keepdims=True) + 1e-06)
    normed = combined * inv_rms
    embedding = normed.astype(jnp.bfloat16).reshape(rows_dev, hidden_width)
    incoming = cotangent.reshape(blocks, block_rows, hidden_width).astype(jnp.float32)
    mixed_grad = inv_rms * (incoming - normed * jnp.mean(incoming * normed, axis=2, keepdims=True))
    agg_grad = (mixed_grad / weight_total).astype(jnp.bfloat16).reshape(rows_dev, hidden_width)
    by_rows = (((0,), (0,)), ((), ()))
    remote_grad = lax.dot_general(
        pool_adjacency[:, :remote_rows], agg_grad, by_rows, preferred_element_type=jnp.float32
    )
    returned = remote_grad.astype(jnp.bfloat16).reshape(members, TILE, hidden_width)
    came_back = lax.all_to_all(returned, "member", split_axis=0, concat_axis=0, tiled=True)
    own_grad = lax.dot_general(
        pool_adjacency[:, remote_rows:], agg_grad, by_rows, preferred_element_type=jnp.float32
    )
    back_to = (
        (served[:, None] == lax.broadcasted_iota(jnp.int32, (1, tiles_dev), 1))
        & (asked_for >= 0)[:, None]
    ).astype(jnp.bfloat16)
    tile_grad = own_grad.reshape(tiles_dev, TILE * hidden_width) + lax.dot_general(
        back_to,
        came_back.reshape(members, TILE * hidden_width),
        by_rows,
        preferred_element_type=jnp.float32,
    )
    message_grad = mixed_grad.reshape(rows_dev, hidden_width) + tile_grad.reshape(
        rows_dev, hidden_width
    )
    pre_grad = jnp.where(preact > 0, message_grad, 0.0).astype(jnp.bfloat16)
    feat_grad = lax.dot_general(
        pre_grad, transform, (((1,), (1,)), ((), ())), preferred_element_type=jnp.float32
    ).astype(jnp.bfloat16)
    partial = lax.dot_general(
        feats, pre_grad, (((0,), (0,)), ((), ())), preferred_element_type=jnp.float32
    )
    factor = 1.0 / math.sqrt(rows_dev * members * groups)
    transform_grad = reduce_rows(partial) * factor
    return (embedding, feat_grad, transform_grad)


def solution(mesh):
    return jax.shard_map(
        on_device,
        mesh=mesh,
        in_specs=(
            P(("group", "member"), None),
            P(),
            P(),
            P(("group", "member"), None),
            P(("group", "member"), None),
            P(("group", "member"), None),
            P(("group", "member"), None),
        ),
        out_specs=(P(("group", "member"), None), P(("group", "member"), None), P("member", None)),
        check_vma=False,
    )
```

```python
import math

import jax
import jax.numpy as jnp
from jax import lax
from jax.sharding import PartitionSpec as P

TILE = 32


def adjacency_of(slot_rows, weights, cand_width):
    columns = lax.broadcasted_iota(jnp.int32, slot_rows.shape + (cand_width,), slot_rows.ndim)
    matched_weights = jnp.where(slot_rows[..., None] == columns, weights[..., None], 0)
    return jnp.sum(matched_weights, axis=-2).astype(jnp.bfloat16)


def xor_pairs(n, bit):
    return [(i, i ^ (1 << bit)) for i in range(n)]


def reduce_rows(part):
    members = lax.axis_size("member")
    groups = lax.axis_size("group")
    core = lax.axis_index("member") % 2
    rows, cols = part.shape
    left, right = part[:, : cols // 2], part[:, cols // 2 :]
    keep = jnp.where(core == 0, left, right)
    send = jnp.where(core == 0, right, left)
    pair_sum = keep + lax.ppermute(send.astype(jnp.bfloat16), "member", xor_pairs(members, 0)).astype(
        jnp.float32
    )
    block = rows // members
    share = block // groups
    chunks = pair_sum.astype(jnp.bfloat16).reshape(members, groups, share, cols // 2)
    chunks = jnp.transpose(chunks, (1, 0, 2, 3)).reshape(groups * members, share, cols // 2)
    got = lax.all_to_all(chunks, ("group", "member"), split_axis=0, concat_axis=0, tiled=True)
    by_half = jnp.sum(
        got.astype(jnp.float32).reshape(groups * members // 2, 2, share, cols // 2), axis=0
    )
    mine = jnp.transpose(by_half, (1, 0, 2)).reshape(share * cols)
    every = lax.all_to_all(
        jnp.broadcast_to(mine, (groups, share * cols)), "group", split_axis=0, concat_axis=0, tiled=True
    )
    return every.reshape(rows // members, cols)


def on_device(feats, transform, bias, tile_list, nbr_slot, nbr_weight, cotangent):
    rows_dev, feat_width = feats.shape
    hidden_width = transform.shape[1]
    blocks, tiles_per = tile_list.shape
    block_rows = rows_dev // blocks
    members = lax.axis_size("member")
    groups = lax.axis_size("group")
    member_here = lax.axis_index("member")
    tiles_dev = rows_dev // TILE
    cand_width = tiles_per * TILE
    preact = jnp.dot(feats, transform, preferred_element_type=jnp.float32) + bias
    message = jnp.maximum(preact, 0.0).astype(jnp.bfloat16)
    own_tiles = message.reshape(tiles_dev, TILE, hidden_width)
    holder = tile_list // tiles_dev
    local_index = tile_list % tiles_dev
    foreign = holder != member_here
    peer_ids = lax.broadcasted_iota(jnp.int32, (1, 1, members), 2)
    matched = (holder[..., None] == peer_ids) & foreign[..., None]
    wanted = jnp.max(jnp.where(matched, local_index[..., None], -1), axis=(0, 1))
    asked_for = lax.all_to_all(
        wanted.reshape(members, 1), "member", split_axis=0, concat_axis=0, tiled=True
    )[:, 0]
    served = jnp.clip(asked_for, 0, tiles_dev - 1)
    remote = lax.all_to_all(own_tiles[served], "member", split_axis=0, concat_axis=0, tiled=True)
    pool_index = jnp.where(foreign, holder, members + local_index)
    pool_rows = (members + tiles_dev) * TILE
    slot_pool_row = (pool_index[:, :, None] * TILE + jnp.arange(TILE, dtype=jnp.int32)).reshape(
        blocks, cand_width
    )
    place = (
        slot_pool_row[:, :, None] == lax.broadcasted_iota(jnp.int32, (1, 1, pool_rows), 2)
    ).astype(jnp.bfloat16)
    slot_rows = nbr_slot.reshape(blocks, block_rows, -1)
    weights = nbr_weight.reshape(blocks, block_rows, -1)
    adjacency = adjacency_of(slot_rows, weights, cand_width)
    pool_adjacency = jnp.einsum(
        "brc,bcp->brp", adjacency, place, preferred_element_type=jnp.float32
    ).astype(jnp.bfloat16)
    remote_rows = members * TILE
    pool_adjacency = pool_adjacency.reshape(rows_dev, pool_rows)
    weight_total = jnp.sum(weights, axis=2).astype(jnp.float32)[..., None]
    gathered = jnp.dot(
        pool_adjacency[:, remote_rows:], message, preferred_element_type=jnp.float32
    ) + jnp.dot(
        pool_adjacency[:, :remote_rows],
        remote.reshape(remote_rows, hidden_width),
        preferred_element_type=jnp.float32,
    )
    combined = gathered.reshape(blocks, block_rows, hidden_width) / weight_total + message.reshape(
        blocks, block_rows, hidden_width
    ).astype(jnp.float32)
    inv_rms = lax.rsqrt(jnp.mean(combined * combined, axis=2, keepdims=True) + 1e-06)
    normed = combined * inv_rms
    embedding = normed.astype(jnp.bfloat16).reshape(rows_dev, hidden_width)
    incoming = cotangent.reshape(blocks, block_rows, hidden_width).astype(jnp.float32)
    mixed_grad = inv_rms * (incoming - normed * jnp.mean(incoming * normed, axis=2, keepdims=True))
    agg_grad = (mixed_grad / weight_total).astype(jnp.bfloat16).reshape(rows_dev, hidden_width)
    by_rows = (((0,), (0,)), ((), ()))
    remote_grad = lax.dot_general(
        pool_adjacency[:, :remote_rows], agg_grad, by_rows, preferred_element_type=jnp.float32
    )
    returned = remote_grad.astype(jnp.bfloat16).reshape(members, TILE, hidden_width)
    came_back = lax.all_to_all(returned, "member", split_axis=0, concat_axis=0, tiled=True)
    own_grad = lax.dot_general(
        pool_adjacency[:, remote_rows:], agg_grad, by_rows, preferred_element_type=jnp.float32
    )
    back_to = (
        (served[:, None] == lax.broadcasted_iota(jnp.int32, (1, tiles_dev), 1))
        & (asked_for >= 0)[:, None]
    ).astype(jnp.bfloat16)
    tile_grad = own_grad.reshape(tiles_dev, TILE, hidden_width) + jnp.einsum(
        "jt,jrh->trh", back_to, came_back, preferred_element_type=jnp.float32
    )
    message_grad = mixed_grad.reshape(rows_dev, hidden_width) + tile_grad.reshape(
        rows_dev, hidden_width
    )
    pre_grad = jnp.where(preact > 0, message_grad, 0.0).astype(jnp.bfloat16)
    feat_grad = lax.dot_general(
        pre_grad, transform, (((1,), (1,)), ((), ())), preferred_element_type=jnp.float32
    ).astype(jnp.bfloat16)
    partial = lax.dot_general(
        feats, pre_grad, (((0,), (0,)), ((), ())), preferred_element_type=jnp.float32
    )
    factor = 1.0 / math.sqrt(rows_dev * members * groups)
    transform_grad = reduce_rows(partial) * factor
    return (embedding, feat_grad, transform_grad)


def solution(mesh):
    return jax.shard_map(
        on_device,
        mesh=mesh,
        in_specs=(
            P(("group", "member"), None),
            P(),
            P(),
            P(("group", "member"), None),
            P(("group", "member"), None),
            P(("group", "member"), None),
            P(("group", "member"), None),
        ),
        out_specs=(P(("group", "member"), None), P(("group", "member"), None), P("member", None)),
        check_vma=False,
    )
```

```python
import math

import jax
import jax.numpy as jnp
from jax import lax
from jax.sharding import PartitionSpec as P

TILE = 32


def adjacency_of(slot_rows, weights, cand_width):
    columns = lax.broadcasted_iota(jnp.int32, slot_rows.shape + (cand_width,), slot_rows.ndim)
    matched_weights = jnp.where(slot_rows[..., None] == columns, weights[..., None], 0)
    return jnp.sum(matched_weights, axis=-2).astype(jnp.bfloat16)


def xor_pairs(n, bit):
    return [(i, i ^ (1 << bit)) for i in range(n)]


def reduce_rows(part):
    members = lax.axis_size("member")
    groups = lax.axis_size("group")
    core = lax.axis_index("member") % 2
    rows, cols = part.shape
    left, right = part[:, : cols // 2], part[:, cols // 2 :]
    keep = jnp.where(core == 0, left, right)
    send = jnp.where(core == 0, right, left)
    pair_sum = keep + lax.ppermute(send.astype(jnp.bfloat16), "member", xor_pairs(members, 0)).astype(
        jnp.float32
    )
    block = rows // members
    share = block // groups
    chunks = pair_sum.astype(jnp.bfloat16).reshape(members, groups, share, cols // 2)
    chunks = jnp.transpose(chunks, (1, 0, 2, 3)).reshape(groups * members, share, cols // 2)
    got = lax.all_to_all(chunks, ("group", "member"), split_axis=0, concat_axis=0, tiled=True)
    by_half = jnp.sum(
        got.astype(jnp.float32).reshape(groups * members // 2, 2, share, cols // 2), axis=0
    )
    mine = jnp.transpose(by_half, (1, 0, 2)).reshape(share * cols)
    every = lax.all_to_all(
        jnp.broadcast_to(mine.astype(jnp.bfloat16), (groups, share * cols)),
        "group",
        split_axis=0,
        concat_axis=0,
        tiled=True,
    )
    return every.astype(jnp.float32).reshape(rows // members, cols)


def on_device(feats, transform, bias, tile_list, nbr_slot, nbr_weight, cotangent):
    rows_dev, feat_width = feats.shape
    hidden_width = transform.shape[1]
    blocks, tiles_per = tile_list.shape
    block_rows = rows_dev // blocks
    members = lax.axis_size("member")
    groups = lax.axis_size("group")
    member_here = lax.axis_index("member")
    tiles_dev = rows_dev // TILE
    cand_width = tiles_per * TILE
    preact = jnp.dot(feats, transform, preferred_element_type=jnp.float32) + bias
    message = jnp.maximum(preact, 0.0).astype(jnp.bfloat16)
    own_tiles = message.reshape(tiles_dev, TILE, hidden_width)
    holder = tile_list // tiles_dev
    local_index = tile_list % tiles_dev
    foreign = holder != member_here
    peer_ids = lax.broadcasted_iota(jnp.int32, (1, 1, members), 2)
    matched = (holder[..., None] == peer_ids) & foreign[..., None]
    wanted = jnp.max(jnp.where(matched, local_index[..., None], -1), axis=(0, 1))
    asked_for = lax.all_to_all(
        wanted.reshape(members, 1), "member", split_axis=0, concat_axis=0, tiled=True
    )[:, 0]
    served = jnp.clip(asked_for, 0, tiles_dev - 1)
    remote = lax.all_to_all(own_tiles[served], "member", split_axis=0, concat_axis=0, tiled=True)
    pool_index = jnp.where(foreign, holder, members + local_index)
    pool_rows = (members + tiles_dev) * TILE
    slot_pool_row = (pool_index[:, :, None] * TILE + jnp.arange(TILE, dtype=jnp.int32)).reshape(
        blocks, cand_width
    )
    place = (
        slot_pool_row[:, :, None] == lax.broadcasted_iota(jnp.int32, (1, 1, pool_rows), 2)
    ).astype(jnp.bfloat16)
    slot_rows = nbr_slot.reshape(blocks, block_rows, -1)
    weights = nbr_weight.reshape(blocks, block_rows, -1)
    adjacency = adjacency_of(slot_rows, weights, cand_width)
    pool_adjacency = jnp.einsum(
        "brc,bcp->brp", adjacency, place, preferred_element_type=jnp.float32
    ).astype(jnp.bfloat16)
    remote_rows = members * TILE
    pool_adjacency = pool_adjacency.reshape(rows_dev, pool_rows)
    weight_total = jnp.sum(weights, axis=2).astype(jnp.float32)[..., None]
    gathered = jnp.dot(
        pool_adjacency[:, remote_rows:], message, preferred_element_type=jnp.float32
    ) + jnp.dot(
        pool_adjacency[:, :remote_rows],
        remote.reshape(remote_rows, hidden_width),
        preferred_element_type=jnp.float32,
    )
    combined = gathered.reshape(blocks, block_rows, hidden_width) / weight_total + message.reshape(
        blocks, block_rows, hidden_width
    ).astype(jnp.float32)
    inv_rms = lax.rsqrt(jnp.mean(combined * combined, axis=2, keepdims=True) + 1e-06)
    normed = combined * inv_rms
    embedding = normed.astype(jnp.bfloat16).reshape(rows_dev, hidden_width)
    incoming = cotangent.reshape(blocks, block_rows, hidden_width).astype(jnp.float32)
    mixed_grad = inv_rms * (incoming - normed * jnp.mean(incoming * normed, axis=2, keepdims=True))
    agg_grad = (mixed_grad / weight_total).astype(jnp.bfloat16).reshape(rows_dev, hidden_width)
    by_rows = (((0,), (0,)), ((), ()))
    remote_grad = lax.dot_general(
        pool_adjacency[:, :remote_rows], agg_grad, by_rows, preferred_element_type=jnp.float32
    )
    returned = remote_grad.astype(jnp.bfloat16).reshape(members, TILE, hidden_width)
    came_back = lax.all_to_all(returned, "member", split_axis=0, concat_axis=0, tiled=True)
    own_grad = lax.dot_general(
        pool_adjacency[:, remote_rows:], agg_grad, by_rows, preferred_element_type=jnp.float32
    )
    back_to = (
        (served[:, None] == lax.broadcasted_iota(jnp.int32, (1, tiles_dev), 1))
        & (asked_for >= 0)[:, None]
    ).astype(jnp.bfloat16)
    tile_grad = own_grad.reshape(tiles_dev, TILE, hidden_width) + jnp.einsum(
        "jt,jrh->trh", back_to, came_back, preferred_element_type=jnp.float32
    )
    message_grad = mixed_grad.reshape(rows_dev, hidden_width) + tile_grad.reshape(
        rows_dev, hidden_width
    )
    pre_grad = jnp.where(preact > 0, message_grad, 0.0).astype(jnp.bfloat16)
    feat_grad = lax.dot_general(
        pre_grad, transform, (((1,), (1,)), ((), ())), preferred_element_type=jnp.float32
    ).astype(jnp.bfloat16)
    partial = lax.dot_general(
        feats, pre_grad, (((0,), (0,)), ((), ())), preferred_element_type=jnp.float32
    )
    factor = 1.0 / math.sqrt(rows_dev * members * groups)
    transform_grad = reduce_rows(partial) * factor
    return (embedding, feat_grad, transform_grad)


def solution(mesh):
    return jax.shard_map(
        on_device,
        mesh=mesh,
        in_specs=(
            P(("group", "member"), None),
            P(),
            P(),
            P(("group", "member"), None),
            P(("group", "member"), None),
            P(("group", "member"), None),
            P(("group", "member"), None),
        ),
        out_specs=(P(("group", "member"), None), P(("group", "member"), None), P("member", None)),
        check_vma=False,
    )
```
